512 devices in a mesh: gx: 32 (over y, x, core), gy: 16 (over z).
Axes of the slice: x: 4, y: 4, z: 16, core: 2. Of those that a mesh axis runs over, the one named last changes fastest.
Arguments:
- diffusivity: float32 [1024, 2048], P('gx', 'gy'), may hold values from 0.25 to 1
- base_humidity: float32 [1024, 2048], P('gx', 'gy'), may hold values from -4 to 4
- coupling: float32 [1024, 2048], P('gx', 'gy'), may hold values from 0.1 to 0.4
- basis_rows: float32 [1024, 64], P('gx'), may hold values from -0.45 to 0.45
- basis_cols: float32 [2048, 32], P('gy'), may hold values from -0.45 to 0.45
- directions: float32 [16, 64, 32], replicated, may hold values from -5 to 5
- send_cell: int32 [32, 16, 32, 8], P('gx', 'gy'), may hold values from 0 to 4095
- send_weight: float32 [32, 16, 32, 8], P('gx', 'gy'), may hold values from 0.1 to 1
- send_count: int32 [32, 16, 32], P('gx', 'gy'), may hold values from 1 to 8, as said below
- owner_gauge: int32 [32, 16, 32, 8], P('gx', 'gy'), may hold values from 0 to 39
- noise_precision: float32 [32, 16, 40], P('gx', 'gy'), may hold values from 1 to 16
Outputs:
- readings: float32 [32, 16, 16, 40], P('gx', 'gy')
- hess_action: float32 [16, 64, 32], replicated
The draws below stay inside these ranges and needn't reach their ends.
Inputs may be any that keep to these rules, and one draw needn't show every extreme that they name: `send_count`: entries from one device to one owner; in every draw, in each row of the gy axis one owner receives exactly 8 from every device. `send_cell`: A local cell index of the sending device. `owner_gauge`: A gauge of the owner.
All inputs are finite; a program needn't handle non-finite values.
Results may differ from the reference program's by a relative error of at most 0.00011.
Values sent between devices are 32-bit elements; how exact they have to be, the bound alone decides.
No kernel may reach another device: no remote copies, remote signals or barrier semaphores. Data moves between devices by JAX's collectives and lax.ppermute only.
A program may use at most 64 MiB of HBM per device.

```python
import math
import jax
import jax.numpy as jnp
from jax import lax

CX = 32
CY = 128
DIRS = 16
MODES_X = 64
MODES_Y = 32
STEPS = 6
SLOT = 8
GAUGES = 40
NX = 1024
NY = 2048
N_GX = 32
N_GY = 16


def draw_send_count(key, part):
    first_key, second_key = jax.random.split(jax.random.fold_in(key, 17))
    counts = jax.random.randint(first_key, (N_GX, N_GY, N_GX), 1, SLOT + 1)
    offset = jax.random.randint(second_key, (), 0, N_GX)
    full_owner = (offset + 3 * jnp.arange(N_GY, dtype=jnp.int32)) % N_GX
    owner_ids = jnp.arange(N_GX, dtype=jnp.int32)[None, None, :]
    is_full = owner_ids == full_owner[None, :, None]
    return jnp.where(is_full, SLOT, counts).astype(jnp.int32)


def set_ends(entries, own_key, low, top_value):
    shape = entries.shape
    spot = [jax.random.randint(jax.random.fold_in(own_key, axis), (), 0, shape[axis]) for axis in range(len(shape))]
    entries = entries.at[tuple(spot)].set(low)
    longest = shape.index(max(shape))
    spot[longest] = (spot[longest] + 1) % shape[longest]
    return entries.at[tuple(spot)].set(top_value)


def shard_levels(stream_key, shape, cuts, smallest, largest):
    level, own = 1.0, jax.random.fold_in(stream_key, 6)
    for position, shards_of in cuts:
        heights = jnp.exp(jax.random.uniform(jax.random.fold_in(own, position), (shards_of,), jnp.float32, smallest / len(cuts), largest / len(cuts)))
        level = level * jnp.repeat(heights, shape[position] // shards_of).reshape([-1 if axis == position else 1 for axis in range(len(shape))])
    return level


def centred(own_key, dims, deviation, bound, shards=(), kind=jnp.bfloat16):
    array = jax.random.normal(own_key, dims, jnp.float32) * deviation
    if len(shards) > 0:
        array = shard_levels(own_key, dims, shards, -0.22, 0.18) * array
    return jnp.clip(array, min=-bound, max=bound).astype(kind)


def setup_inputs(seed: int = 0) -> dict:
    keys = jax.random.split(jax.random.key(seed), 12)
    return {
        "diffusivity": jnp.clip(jnp.exp(math.log(1.0) - 1.3862944 * jax.random.uniform(keys[0], (NX, NY), jnp.float32) ** shard_levels(keys[0], (NX, NY), ((0, 32), (1, 16)), -0.2, 0.2)), 0.25, 1.0),
        "base_humidity": centred(keys[1], (NX, NY), 1.0, 4.0, ((0, 32), (1, 16)), jnp.float32),
        "coupling": jnp.clip(jnp.exp(math.log(0.4) - 1.3862944 * jax.random.uniform(keys[2], (NX, NY), jnp.float32) ** shard_levels(keys[2], (NX, NY), ((0, 32), (1, 16)), -0.2, 0.2)), 0.1, 0.4),
        "basis_rows": centred(keys[3], (NX, MODES_X), 0.075, 0.45, ((0, 32),), jnp.float32),
        "basis_cols": centred(keys[4], (NY, MODES_Y), 0.075, 0.45, ((0, 16),), jnp.float32),
        "directions": centred(keys[5], (DIRS, MODES_X, MODES_Y), 1.0, 5.0, (), jnp.float32),
        "send_cell": set_ends(jax.random.randint(keys[6], (N_GX, N_GY, N_GX, SLOT), 0, CX * CY), jax.random.fold_in(keys[6], 1), 0, (CX * CY) - 1).astype(jnp.int32),
        "send_weight": jnp.clip(0.1 + 0.9 * jax.random.uniform(keys[7], (N_GX, N_GY, N_GX, SLOT), jnp.float32) ** shard_levels(keys[7], (N_GX, N_GY, N_GX, SLOT), ((0, 32), (1, 16)), -0.2, 0.2), 0.1, 1.0),
        "send_count": draw_send_count(jax.random.fold_in(keys[11], 71), 0),
        "owner_gauge": set_ends(jax.random.randint(keys[9], (N_GX, N_GY, N_GX, SLOT), 0, GAUGES), jax.random.fold_in(keys[9], 1), 0, GAUGES - 1).astype(jnp.int32),
        "noise_precision": jnp.clip(jnp.exp(math.log(16.0) - 2.7725887 * jax.random.uniform(keys[10], (N_GX, N_GY, GAUGES), jnp.float32) ** shard_levels(keys[10], (N_GX, N_GY, GAUGES), ((0, 32), (1, 16)), -0.2, 0.2)), 1.0, 16.0),
    }


step_ratio = 0.2
exact = lax.Precision.HIGHEST


def bordered(field):
    return jnp.pad(field, [(0, 0)] * (field.ndim - 2) + [(1, 1), (1, 1)])


def spread(field):
    middle = field[..., 1:-1, 1:-1]
    return middle, (field[..., :-2, 1:-1], field[..., 2:, 1:-1], field[..., 1:-1, :-2], field[..., 1:-1, 2:])


def update(temper, humid, diff_pad, coupling, orient):
    temp_mid, temp_near = spread(bordered(temper))
    hum_mid, hum_near = spread(bordered(humid))
    diff_mid, diff_near = spread(diff_pad)
    lap_temp = sum(n - temp_mid for n in temp_near)
    lap_hum = sum(0.5 * (diff_mid + k) * (n - hum_mid) for k, n in zip(diff_near, hum_near))
    new_temp = temp_mid + step_ratio * lap_temp + orient * coupling * hum_mid
    new_hum = hum_mid + step_ratio * lap_hum - orient * coupling * temp_mid
    return new_temp, new_hum


def reference(diffusivity, base_humidity, coupling, basis_rows, basis_cols, directions, send_cell, send_weight, send_count, owner_gauge, noise_precision):
    sender = jnp.arange(N_GX, dtype=jnp.int32)[:, None, None, None]
    column_dev = jnp.arange(N_GY, dtype=jnp.int32)[None, :, None, None]
    owner = jnp.arange(N_GX, dtype=jnp.int32)[None, None, :, None]
    slot_idx = jnp.arange(SLOT, dtype=jnp.int32)[None, None, None, :]
    row_global = sender * CX + send_cell // CY
    col_global = column_dev * CY + send_cell % CY
    cell_index = (row_global * NY + col_global).reshape(-1).astype(jnp.int32)
    live_mask = (slot_idx < send_count[..., None]).astype(jnp.float32)
    factor = (send_weight * live_mask).reshape(-1)
    gauge_sent = jnp.transpose(owner_gauge, (2, 1, 0, 3))
    gauge_index = ((owner * N_GY + column_dev) * GAUGES + gauge_sent).reshape(-1).astype(jnp.int32)
    diff_pad = bordered(diffusivity)
    hum_pad = bordered(base_humidity)
    hum_mid, hum_near = spread(hum_pad)
    weights_flat = noise_precision.reshape(-1)

    def one_direction(vector):
        perturb = jnp.dot(jnp.dot(basis_rows, vector, precision=exact), basis_cols.T, precision=exact)
        param_mid, param_near = spread(bordered(diffusivity * perturb))
        source = sum(0.5 * (param_mid + p) * (h - hum_mid) for p, h in zip(param_near, hum_near))
        temper = jnp.zeros_like(source)
        humid = step_ratio * source
        for i in range(STEPS - 1):
            temper, humid = update(temper, humid, diff_pad, coupling, 1.0)
            humid = humid + step_ratio * source
        picked = humid.reshape(-1)[cell_index] * factor
        gauge_read = jax.ops.segment_sum(picked, gauge_index, num_segments=N_GX * N_GY * GAUGES)
        weighted = weights_flat * gauge_read
        returned = weighted[gauge_index] * factor
        adjoint_load = jax.ops.segment_sum(returned, cell_index, num_segments=NX * NY).reshape(NX, NY)
        adj_temp = jnp.zeros_like(adjoint_load)
        adj_hum = adjoint_load
        summed = adjoint_load
        for i in range(STEPS - 1):
            adj_temp, adj_hum = update(adj_temp, adj_hum, diff_pad, coupling, -1.0)
            summed = summed + adj_hum
        lam_field = step_ratio * summed
        lam_mid, lam_near = spread(bordered(lam_field))
        gradient = diffusivity * sum(0.5 * (h - hum_mid) * (lam_mid - l) for h, l in zip(hum_near, lam_near))
        projected = jnp.dot(jnp.dot(basis_rows.T, gradient, precision=exact), basis_cols, precision=exact)
        return gauge_read, vector + projected

    gauge_all, hess_action = lax.map(one_direction, directions)
    readings = jnp.transpose(gauge_all.reshape(DIRS, N_GX, N_GY, GAUGES), (1, 2, 0, 3))
    return readings, hess_action
```

```python
import jax
import jax.numpy as jnp
from jax import lax
from jax.sharding import PartitionSpec as P

STEPS = 6


step_ratio = 0.2
exact = lax.Precision.HIGHEST


def extended(cells, sides, width):
    for axis, dim in sides:
        count = lax.axis_size(axis)
        ends = count - 1
        head = lax.slice_in_dim(cells, 0, width, axis=dim)
        tail = lax.slice_in_dim(cells, cells.shape[dim] - width, cells.shape[dim], axis=dim)
        cells = jnp.concatenate(
            [
                lax.ppermute(tail, axis, [(i, (i + 1) % count) for i in range(ends)]),
                cells,
                lax.ppermute(head, axis, [((i + 1) % count, i) for i in range(ends)]),
            ],
            axis=dim,
        )
    return cells


def spread(field):
    middle = field[..., 1:-1, 1:-1]
    return (
        middle,
        (field[..., :-2, 1:-1], field[..., 2:, 1:-1], field[..., 1:-1, :-2], field[..., 1:-1, 2:]),
    )


def window(field, have, want):
    offset = have - want
    return field[..., offset : field.shape[-2] - offset, offset : field.shape[-1] - offset]


def advance(state_now, static_pad, orient):
    temp_mid, temp_near = spread(state_now[0])
    hum_mid, hum_near = spread(state_now[1])
    diff_mid, diff_near = spread(static_pad[0])
    couple_mid = static_pad[2, 1:-1, 1:-1]
    inside = static_pad[3, 1:-1, 1:-1]
    lap_temp = sum((n - temp_mid for n in temp_near))
    lap_hum = sum((0.5 * (diff_mid + k) * (n - hum_mid) for k, n in zip(diff_near, hum_near)))
    new_temp = temp_mid + step_ratio * lap_temp + orient * couple_mid * hum_mid
    new_hum = hum_mid + step_ratio * lap_hum - orient * couple_mid * temp_mid
    return jnp.stack([new_temp * inside, new_hum * inside])


def make_source(param_pad, static_pad):
    param_mid, param_near = spread(param_pad)
    hum_mid, hum_near = spread(static_pad[1])
    inside = static_pad[3, 1:-1, 1:-1]
    return (
        sum((0.5 * (param_mid + p) * (h - hum_mid) for p, h in zip(param_near, hum_near))) * inside
    )


def state_rim(state_now):
    return extended(state_now, (("gx", 2), ("gy", 3)), 1)


def butterfly(values, axis):
    count = lax.axis_size(axis)
    stride = 1
    while stride < count:
        values = values + lax.ppermute(values, axis, [(i, i ^ stride) for i in range(count)])
        stride *= 2
    return values


def local(
    diffusivity,
    base_humidity,
    coupling,
    basis_rows,
    basis_cols,
    directions,
    send_cell,
    send_weight,
    send_count,
    owner_gauge,
    noise_precision,
):
    rim_depth = STEPS
    height, breadth = diffusivity.shape
    n_dirs = directions.shape[0]
    static = jnp.stack([diffusivity, base_humidity, coupling, jnp.ones_like(diffusivity)])
    static_wide = extended(static, (("gx", 1), ("gy", 2)), rim_depth)
    static_near = window(static_wide, rim_depth, 1)
    rows_wide = extended(basis_rows, (("gx", 0),), rim_depth)
    cols_wide = extended(basis_cols, (("gy", 0),), rim_depth)
    perturb = jnp.einsum("xa,rab->rxb", rows_wide, directions, precision=exact)
    perturb = jnp.einsum("rxb,yb->rxy", perturb, cols_wide, precision=exact)
    param_wide = static_wide[0] * perturb
    source = make_source(param_wide, static_wide)
    src_depth = rim_depth - 1
    state_now = jnp.stack([jnp.zeros_like(source), step_ratio * source])
    for i in range(rim_depth - 1):
        depth = src_depth - i
        state_now = advance(state_now, window(static_wide, rim_depth, depth), 1.0)
        state_now = jnp.stack(
            [state_now[0], state_now[1] + step_ratio * window(source, src_depth, depth - 1)]
        )
    humid = state_now[1]
    peers = send_cell.shape[2]
    slots = send_cell.shape[3]
    gauges = noise_precision.shape[2]
    cell_ids = send_cell.reshape(-1)
    live_mask = (
        lax.broadcasted_iota(jnp.int32, (peers, slots), 1) < send_count.reshape(peers, 1)
    ).astype(jnp.float32)
    factor = send_weight.reshape(peers, slots) * live_mask
    picked = (
        jnp.take(humid.reshape(n_dirs, height * breadth), cell_ids, axis=1).reshape(
            n_dirs, peers, slots
        )
        * factor
    )
    gauge_ids = owner_gauge.reshape(-1)
    lookup = (gauge_ids[:, None] == lax.broadcasted_iota(jnp.int32, (1, gauges), 1)).astype(
        jnp.float32
    )
    gauge_weights = noise_precision.reshape(1, gauges)
    arrived = lax.all_to_all(picked, "gx", split_axis=1, concat_axis=1, tiled=True)
    n_items = arrived.shape[0]
    gauge_read = jnp.dot(arrived.reshape(n_items, peers * slots), lookup, precision=exact)
    backward = jnp.dot(gauge_read * gauge_weights, lookup.T, precision=exact).reshape(
        n_items, peers, slots
    )
    returned = lax.all_to_all(backward, "gx", split_axis=1, concat_axis=1, tiled=True)
    load_values = (returned * factor).reshape(n_dirs, peers * slots)
    adjoint_load = (
        jnp.zeros((n_dirs, height * breadth), jnp.float32).at[:, cell_ids].add(load_values)
    )
    adjoint_load = adjoint_load.reshape(n_dirs, height, breadth)
    load_wide = extended(adjoint_load, (("gx", 1), ("gy", 2)), rim_depth)
    state_now = jnp.stack([jnp.zeros_like(load_wide), load_wide])
    summed = window(load_wide, rim_depth, 1)
    for i in range(rim_depth - 1):
        depth = rim_depth - i
        state_now = advance(state_now, window(static_wide, rim_depth, depth), -1.0)
        summed = summed + window(state_now[1], depth - 1, 1)
    lam_wide = step_ratio * summed
    lam_mid, lam_near = spread(lam_wide)
    hum_mid, hum_near = spread(static_near[1])
    gradient = diffusivity * sum(
        (0.5 * (h - hum_mid) * (lam_mid - l) for h, l in zip(hum_near, lam_near))
    )
    projected = jnp.einsum("rxy,yb->rxb", gradient, basis_cols, precision=exact)
    projected = jnp.einsum("xa,rxb->rab", basis_rows, projected, precision=exact).reshape(
        n_dirs, -1
    )
    summed_modes = butterfly(butterfly(projected, "gx"), "gy")
    hess_action = directions + summed_modes.reshape(directions.shape)
    return (gauge_read.reshape(1, 1, n_dirs, gauges), hess_action)


def solution(mesh):
    placed = (
        P("gx", "gy"),
        P("gx", "gy"),
        P("gx", "gy"),
        P("gx", None),
        P("gy", None),
        P(),
        P("gx", "gy", None, None),
        P("gx", "gy", None, None),
        P("gx", "gy", None),
        P("gx", "gy", None, None),
        P("gx", "gy", None),
    )
    return jax.shard_map(
        local,
        mesh=mesh,
        in_specs=placed,
        out_specs=(P("gx", "gy", None, None), P()),
        check_vma=False,
    )
```

```python
import jax
import jax.numpy as jnp
from jax import lax
from jax.sharding import PartitionSpec as P

STEPS = 6


step_ratio = 0.2
exact = lax.Precision.HIGHEST


def extended(cells, sides, width):
    for axis, dim in sides:
        count = lax.axis_size(axis)
        ends = count - 1
        head = lax.slice_in_dim(cells, 0, width, axis=dim)
        tail = lax.slice_in_dim(cells, cells.shape[dim] - width, cells.shape[dim], axis=dim)
        cells = jnp.concatenate(
            [
                lax.ppermute(tail, axis, [(i, (i + 1) % count) for i in range(ends)]),
                cells,
                lax.ppermute(head, axis, [((i + 1) % count, i) for i in range(ends)]),
            ],
            axis=dim,
        )
    return cells


def spread(field):
    middle = field[..., 1:-1, 1:-1]
    return (
        middle,
        (field[..., :-2, 1:-1], field[..., 2:, 1:-1], field[..., 1:-1, :-2], field[..., 1:-1, 2:]),
    )


def window(field, have, want):
    offset = have - want
    return field[..., offset : field.shape[-2] - offset, offset : field.shape[-1] - offset]


def advance(state_now, static_pad, orient):
    temp_mid, temp_near = spread(state_now[0])
    hum_mid, hum_near = spread(state_now[1])
    diff_mid, diff_near = spread(static_pad[0])
    couple_mid = static_pad[2, 1:-1, 1:-1]
    inside = static_pad[3, 1:-1, 1:-1]
    lap_temp = sum((n - temp_mid for n in temp_near))
    lap_hum = sum((0.5 * (diff_mid + k) * (n - hum_mid) for k, n in zip(diff_near, hum_near)))
    new_temp = temp_mid + step_ratio * lap_temp + orient * couple_mid * hum_mid
    new_hum = hum_mid + step_ratio * lap_hum - orient * couple_mid * temp_mid
    return jnp.stack([new_temp * inside, new_hum * inside])


def make_source(param_pad, static_pad):
    param_mid, param_near = spread(param_pad)
    hum_mid, hum_near = spread(static_pad[1])
    inside = static_pad[3, 1:-1, 1:-1]
    return (
        sum((0.5 * (param_mid + p) * (h - hum_mid) for p, h in zip(param_near, hum_near))) * inside
    )


def state_rim(state_now):
    return extended(state_now, (("gx", 2), ("gy", 3)), 1)


def exchange(parts, axis, width):
    count = lax.axis_size(axis)
    ends = count - 1
    heads = [lax.slice_in_dim(a, 0, width, axis=d) for a, d in parts]
    tails = [lax.slice_in_dim(a, a.shape[d] - width, a.shape[d], axis=d) for a, d in parts]

    def pack(pieces):
        return jnp.concatenate([p.reshape(-1) for p in pieces])

    def unpack(flat, like):
        out, offset = [], 0
        for p in like:
            out.append(flat[offset : offset + p.size].reshape(p.shape))
            offset += p.size
        return out

    from_prev = unpack(lax.ppermute(pack(tails), axis, [(i, i + 1) for i in range(ends)]), tails)
    from_next = unpack(lax.ppermute(pack(heads), axis, [(i + 1, i) for i in range(ends)]), heads)
    return [
        jnp.concatenate([p, a, n], axis=d) for (a, d), p, n in zip(parts, from_prev, from_next)
    ]


def butterfly(values, axis):
    count = lax.axis_size(axis)
    stride = 1
    while stride < count:
        values = values + lax.ppermute(values, axis, [(i, i ^ stride) for i in range(count)])
        stride *= 2
    return values


def all_sum(values):
    count = lax.axis_size("gx")
    flat = values.reshape(count, -1, 128)
    part = lax.all_to_all(flat, "gx", 0, 0, tiled=True).sum(0)
    part = butterfly(part, "gy")
    spread_out = jnp.broadcast_to(part[None], (count,) + part.shape)
    return lax.all_to_all(spread_out, "gx", 0, 0, tiled=True).reshape(values.shape)


def pad_sides(field, width):
    return jnp.pad(field, [(0, 0)] * (field.ndim - 2) + [(width, width), (width, width)])


def local(
    diffusivity,
    base_humidity,
    coupling,
    basis_rows,
    basis_cols,
    directions,
    send_cell,
    send_weight,
    send_count,
    owner_gauge,
    noise_precision,
):
    rim_depth = STEPS
    reach = rim_depth + 1
    height, breadth = diffusivity.shape
    n_dirs = directions.shape[0]
    static = jnp.stack([diffusivity, base_humidity, coupling, jnp.ones_like(diffusivity)])
    static_gx, rows_wide = exchange(((static, 1), (basis_rows, 0)), "gx", reach)
    static_wide, cols_wide = exchange(((static_gx, 2), (basis_cols, 0)), "gy", reach)
    static_six = window(static_wide, reach, rim_depth)
    rows_six = rows_wide[1:-1]
    cols_six = cols_wide[1:-1]
    perturb = jnp.einsum("xa,rab->rxb", rows_six, directions, precision=exact)
    perturb = jnp.einsum("rxb,yb->rxy", perturb, cols_six, precision=exact)
    param_wide = static_six[0] * perturb
    source = make_source(param_wide, static_six)
    src_depth = rim_depth - 1
    state_now = jnp.stack([jnp.zeros_like(source), step_ratio * source])
    for i in range(rim_depth - 1):
        depth = src_depth - i
        state_now = advance(state_now, window(static_wide, reach, depth), 1.0)
        state_now = jnp.stack(
            [state_now[0], state_now[1] + step_ratio * window(source, src_depth, depth - 1)]
        )
    humid = state_now[1]
    peers = send_cell.shape[2]
    slots = send_cell.shape[3]
    gauges = noise_precision.shape[2]
    cell_ids = send_cell.reshape(-1)
    live_mask = (
        lax.broadcasted_iota(jnp.int32, (peers, slots), 1) < send_count.reshape(peers, 1)
    ).astype(jnp.float32)
    factor = send_weight.reshape(peers, slots) * live_mask
    picked = (
        jnp.take(humid.reshape(n_dirs, height * breadth), cell_ids, axis=1).reshape(
            n_dirs, peers, slots
        )
        * factor
    )
    gauge_ids = owner_gauge.reshape(-1)
    lookup = (gauge_ids[:, None] == lax.broadcasted_iota(jnp.int32, (1, gauges), 1)).astype(
        jnp.float32
    )
    gauge_weights = noise_precision.reshape(1, gauges)
    arrived = lax.all_to_all(picked, "gx", split_axis=1, concat_axis=1, tiled=True)
    n_items = arrived.shape[0]
    gauge_read = jnp.dot(arrived.reshape(n_items, peers * slots), lookup, precision=exact)
    backward = jnp.dot(gauge_read * gauge_weights, lookup.T, precision=exact).reshape(
        n_items, peers, slots
    )
    returned = lax.all_to_all(backward, "gx", split_axis=1, concat_axis=1, tiled=True)
    load_values = (returned * factor).reshape(n_dirs, peers * slots)
    adjoint_load = (
        jnp.zeros((n_dirs, height * breadth), jnp.float32).at[:, cell_ids].add(load_values)
    )
    load_wide = pad_sides(adjoint_load.reshape(n_dirs, height, breadth), rim_depth)
    state_now = jnp.stack([jnp.zeros_like(load_wide), load_wide])
    summed = load_wide
    for i in range(rim_depth - 1):
        state_now = pad_sides(advance(state_now, static_six, -1.0), 1)
        summed = summed + state_now[1]
    lam_wide = pad_sides(step_ratio * summed, 1)
    lam_mid, lam_near = spread(lam_wide)
    hum_mid, hum_near = spread(static_wide[1])
    gradient = static_six[0] * sum(
        (0.5 * (h - hum_mid) * (lam_mid - l) for h, l in zip(hum_near, lam_near))
    )
    projected = jnp.einsum("rxy,yb->rxb", gradient, cols_six, precision=exact)
    projected = jnp.einsum("xa,rxb->rab", rows_six, projected, precision=exact)
    summed_modes = all_sum(projected.reshape(n_dirs, -1))
    hess_action = directions + summed_modes.reshape(directions.shape)
    return (gauge_read.reshape(1, 1, n_dirs, gauges), hess_action)


def solution(mesh):
    placed = (
        P("gx", "gy"),
        P("gx", "gy"),
        P("gx", "gy"),
        P("gx", None),
        P("gy", None),
        P(),
        P("gx", "gy", None, None),
        P("gx", "gy", None, None),
        P("gx", "gy", None),
        P("gx", "gy", None, None),
        P("gx", "gy", None),
    )
    return jax.shard_map(
        local,
        mesh=mesh,
        in_specs=placed,
        out_specs=(P("gx", "gy", None, None), P()),
        check_vma=False,
    )
```

```python
import jax
import jax.numpy as jnp
from jax import lax
from jax.sharding import PartitionSpec as P

STEPS = 6


step_ratio = 0.2
exact = lax.Precision.HIGHEST


def extended(cells, sides, width):
    for axis, dim in sides:
        count = lax.axis_size(axis)
        ends = count - 1
        head = lax.slice_in_dim(cells, 0, width, axis=dim)
        tail = lax.slice_in_dim(cells, cells.shape[dim] - width, cells.shape[dim], axis=dim)
        cells = jnp.concatenate(
            [
                lax.ppermute(tail, axis, [(i, (i + 1) % count) for i in range(ends)]),
                cells,
                lax.ppermute(head, axis, [((i + 1) % count, i) for i in range(ends)]),
            ],
            axis=dim,
        )
    return cells


def spread(field):
    middle = field[..., 1:-1, 1:-1]
    return (
        middle,
        (field[..., :-2, 1:-1], field[..., 2:, 1:-1], field[..., 1:-1, :-2], field[..., 1:-1, 2:]),
    )


def window(field, have, want):
    offset = have - want
    return field[..., offset : field.shape[-2] - offset, offset : field.shape[-1] - offset]


def advance(state_now, static_pad, orient):
    temp_mid, temp_near = spread(state_now[0])
    hum_mid, hum_near = spread(state_now[1])
    diff_mid, diff_near = spread(static_pad[0])
    couple_mid = static_pad[2, 1:-1, 1:-1]
    inside = static_pad[3, 1:-1, 1:-1]
    lap_temp = sum((n - temp_mid for n in temp_near))
    lap_hum = sum((0.5 * (diff_mid + k) * (n - hum_mid) for k, n in zip(diff_near, hum_near)))
    new_temp = temp_mid + step_ratio * lap_temp + orient * couple_mid * hum_mid
    new_hum = hum_mid + step_ratio * lap_hum - orient * couple_mid * temp_mid
    return jnp.stack([new_temp * inside, new_hum * inside])


def make_source(param_pad, static_pad):
    param_mid, param_near = spread(param_pad)
    hum_mid, hum_near = spread(static_pad[1])
    inside = static_pad[3, 1:-1, 1:-1]
    return (
        sum((0.5 * (param_mid + p) * (h - hum_mid) for p, h in zip(param_near, hum_near))) * inside
    )


def state_rim(state_now):
    return extended(state_now, (("gx", 2), ("gy", 3)), 1)


def all_sum(values):
    count = lax.axis_size("gx")
    rows = lax.axis_size("gy")
    flat = values.reshape(count, -1, 128)
    part = lax.all_to_all(flat, "gx", 0, 0, tiled=True).sum(0)
    copies = jnp.broadcast_to(part[None], (rows,) + part.shape)
    part = lax.all_to_all(copies, "gy", 0, 0, tiled=True).sum(0)
    spread_out = jnp.broadcast_to(part[None], (count,) + part.shape)
    return lax.all_to_all(spread_out, "gx", 0, 0, tiled=True).reshape(values.shape)


def halo_round(static, rows, cols, width):
    n_gx = lax.axis_size("gx")
    n_gy = lax.axis_size("gy")
    w = width

    def corner(block, step_x, step_y):
        pairs = []
        for a in range(n_gx):
            for b in range(n_gy):
                if 0 <= a + step_x < n_gx and 0 <= b + step_y < n_gy:
                    pairs.append((a * n_gy + b, (a + step_x) * n_gy + b + step_y))
        return lax.ppermute(block, ("gx", "gy"), pairs)

    (_, up, down), (row_up, row_down) = edge_pair(((static, 1), (rows, 0)), "gx", w)
    (_, left, right), (col_left, col_right) = edge_pair(((static, 2), (cols, 0)), "gy", w)
    up_left = corner(static[:, -w:, -w:], 1, 1)
    up_right = corner(static[:, -w:, :w], 1, -1)
    down_left = corner(static[:, :w, -w:], -1, 1)
    down_right = corner(static[:, :w, :w], -1, -1)
    top = jnp.concatenate([up_left, up, up_right], axis=2)
    middle = jnp.concatenate([left, static, right], axis=2)
    bottom = jnp.concatenate([down_left, down, down_right], axis=2)
    wide = jnp.concatenate([top, middle, bottom], axis=1)
    rows_wide = jnp.concatenate([row_up, rows, row_down], axis=0)
    cols_wide = jnp.concatenate([col_left, cols, col_right], axis=0)
    return wide, rows_wide, cols_wide


def edge_pair(parts, axis, width):
    count = lax.axis_size(axis)
    ends = count - 1
    heads = [lax.slice_in_dim(a, 0, width, axis=d) for a, d in parts]
    tails = [lax.slice_in_dim(a, a.shape[d] - width, a.shape[d], axis=d) for a, d in parts]

    def pack(pieces):
        return jnp.concatenate([p.reshape(-1) for p in pieces])

    def unpack(flat, like):
        out, offset = [], 0
        for p in like:
            out.append(flat[offset : offset + p.size].reshape(p.shape))
            offset += p.size
        return out

    from_prev = unpack(lax.ppermute(pack(tails), axis, [(i, i + 1) for i in range(ends)]), tails)
    from_next = unpack(lax.ppermute(pack(heads), axis, [(i + 1, i) for i in range(ends)]), heads)
    return (None, from_prev[0], from_next[0]), (from_prev[1], from_next[1])


def pad_sides(field, width):
    return jnp.pad(field, [(0, 0)] * (field.ndim - 2) + [(width, width), (width, width)])


def local(
    diffusivity,
    base_humidity,
    coupling,
    basis_rows,
    basis_cols,
    directions,
    send_cell,
    send_weight,
    send_count,
    owner_gauge,
    noise_precision,
):
    rim_depth = STEPS
    reach = rim_depth + 1
    height, breadth = diffusivity.shape
    n_dirs = directions.shape[0]
    static = jnp.stack([diffusivity, base_humidity, coupling, jnp.ones_like(diffusivity)])
    static_wide, rows_wide, cols_wide = halo_round(static, basis_rows, basis_cols, reach)
    static_six = window(static_wide, reach, rim_depth)
    rows_six = rows_wide[1:-1]
    cols_six = cols_wide[1:-1]
    perturb = jnp.einsum("xa,rab->rxb", rows_six, directions, precision=exact)
    perturb = jnp.einsum("rxb,yb->rxy", perturb, cols_six, precision=exact)
    param_wide = static_six[0] * perturb
    source = make_source(param_wide, static_six)
    src_depth = rim_depth - 1
    state_now = jnp.stack([jnp.zeros_like(source), step_ratio * source])
    for i in range(rim_depth - 1):
        depth = src_depth - i
        state_now = advance(state_now, window(static_wide, reach, depth), 1.0)
        state_now = jnp.stack(
            [state_now[0], state_now[1] + step_ratio * window(source, src_depth, depth - 1)]
        )
    humid = state_now[1]
    peers = send_cell.shape[2]
    slots = send_cell.shape[3]
    gauges = noise_precision.shape[2]
    cell_ids = send_cell.reshape(-1)
    live_mask = (
        lax.broadcasted_iota(jnp.int32, (peers, slots), 1) < send_count.reshape(peers, 1)
    ).astype(jnp.float32)
    factor = send_weight.reshape(peers, slots) * live_mask
    picked = (
        jnp.take(humid.reshape(n_dirs, height * breadth), cell_ids, axis=1).reshape(
            n_dirs, peers, slots
        )
        * factor
    )
    gauge_ids = owner_gauge.reshape(-1)
    lookup = (gauge_ids[:, None] == lax.broadcasted_iota(jnp.int32, (1, gauges), 1)).astype(
        jnp.float32
    )
    gauge_weights = noise_precision.reshape(1, gauges)
    arrived = lax.all_to_all(picked, "gx", split_axis=1, concat_axis=1, tiled=True)
    n_items = arrived.shape[0]
    gauge_read = jnp.dot(arrived.reshape(n_items, peers * slots), lookup, precision=exact)
    backward = jnp.dot(gauge_read * gauge_weights, lookup.T, precision=exact).reshape(
        n_items, peers, slots
    )
    returned = lax.all_to_all(backward, "gx", split_axis=1, concat_axis=1, tiled=True)
    load_values = (returned * factor).reshape(n_dirs, peers * slots)
    adjoint_load = (
        jnp.zeros((n_dirs, height * breadth), jnp.float32).at[:, cell_ids].add(load_values)
    )
    load_wide = pad_sides(adjoint_load.reshape(n_dirs, height, breadth), rim_depth)
    state_now = jnp.stack([jnp.zeros_like(load_wide), load_wide])
    summed = load_wide
    for i in range(rim_depth - 1):
        state_now = pad_sides(advance(state_now, static_six, -1.0), 1)
        summed = summed + state_now[1]
    lam_wide = pad_sides(step_ratio * summed, 1)
    lam_mid, lam_near = spread(lam_wide)
    hum_mid, hum_near = spread(static_wide[1])
    gradient = static_six[0] * sum(
        (0.5 * (h - hum_mid) * (lam_mid - l) for h, l in zip(hum_near, lam_near))
    )
    projected = jnp.einsum("rxy,yb->rxb", gradient, cols_six, precision=exact)
    projected = jnp.einsum("xa,rxb->rab", rows_six, projected, precision=exact)
    summed_modes = all_sum(projected.reshape(n_dirs, -1))
    hess_action = directions + summed_modes.reshape(directions.shape)
    return (gauge_read.reshape(1, 1, n_dirs, gauges), hess_action)


def solution(mesh):
    placed = (
        P("gx", "gy"),
        P("gx", "gy"),
        P("gx", "gy"),
        P("gx", None),
        P("gy", None),
        P(),
        P("gx", "gy", None, None),
        P("gx", "gy", None, None),
        P("gx", "gy", None),
        P("gx", "gy", None, None),
        P("gx", "gy", None),
    )
    return jax.shard_map(
        local,
        mesh=mesh,
        in_specs=placed,
        out_specs=(P("gx", "gy", None, None), P()),
        check_vma=False,
    )
```

```python
import jax
import jax.numpy as jnp
from jax import lax
from jax.sharding import PartitionSpec as P

STEPS = 6


step_ratio = 0.2
exact = lax.Precision.HIGHEST


def extended(cells, sides, width):
    for axis, dim in sides:
        count = lax.axis_size(axis)
        ends = count - 1
        head = lax.slice_in_dim(cells, 0, width, axis=dim)
        tail = lax.slice_in_dim(cells, cells.shape[dim] - width, cells.shape[dim], axis=dim)
        cells = jnp.concatenate(
            [
                lax.ppermute(tail, axis, [(i, (i + 1) % count) for i in range(ends)]),
                cells,
                lax.ppermute(head, axis, [((i + 1) % count, i) for i in range(ends)]),
            ],
            axis=dim,
        )
    return cells


def spread(field):
    middle = field[..., 1:-1, 1:-1]
    return (
        middle,
        (field[..., :-2, 1:-1], field[..., 2:, 1:-1], field[..., 1:-1, :-2], field[..., 1:-1, 2:]),
    )


def window(field, have, want):
    offset = have - want
    return field[..., offset : field.shape[-2] - offset, offset : field.shape[-1] - offset]


def advance(state_now, static_pad, orient):
    temp_mid, temp_near = spread(state_now[0])
    hum_mid, hum_near = spread(state_now[1])
    diff_mid, diff_near = spread(static_pad[0])
    couple_mid = static_pad[2, 1:-1, 1:-1]
    inside = static_pad[3, 1:-1, 1:-1]
    lap_temp = sum((n - temp_mid for n in temp_near))
    lap_hum = sum((0.5 * (diff_mid + k) * (n - hum_mid) for k, n in zip(diff_near, hum_near)))
    new_temp = temp_mid + step_ratio * lap_temp + orient * couple_mid * hum_mid
    new_hum = hum_mid + step_ratio * lap_hum - orient * couple_mid * temp_mid
    return jnp.stack([new_temp * inside, new_hum * inside])


def make_source(param_pad, static_pad):
    param_mid, param_near = spread(param_pad)
    hum_mid, hum_near = spread(static_pad[1])
    inside = static_pad[3, 1:-1, 1:-1]
    return (
        sum((0.5 * (param_mid + p) * (h - hum_mid) for p, h in zip(param_near, hum_near))) * inside
    )


def state_rim(state_now):
    return extended(state_now, (("gx", 2), ("gy", 3)), 1)


def exchange(parts, axis, width):
    count = lax.axis_size(axis)
    ends = count - 1
    heads = [lax.slice_in_dim(a, 0, width, axis=d) for a, d in parts]
    tails = [lax.slice_in_dim(a, a.shape[d] - width, a.shape[d], axis=d) for a, d in parts]

    def pack(pieces):
        return jnp.concatenate([p.reshape(-1) for p in pieces])

    def unpack(flat, like):
        out, offset = [], 0
        for p in like:
            out.append(flat[offset : offset + p.size].reshape(p.shape))
            offset += p.size
        return out

    from_prev = unpack(lax.ppermute(pack(tails), axis, [(i, i + 1) for i in range(ends)]), tails)
    from_next = unpack(lax.ppermute(pack(heads), axis, [(i + 1, i) for i in range(ends)]), heads)
    return [
        jnp.concatenate([p, a, n], axis=d) for (a, d), p, n in zip(parts, from_prev, from_next)
    ]


def all_sum(values):
    count = lax.axis_size("gx")
    rows = lax.axis_size("gy")
    flat = values.reshape(count, -1, 128)
    part = lax.all_to_all(flat, "gx", 0, 0, tiled=True).sum(0)
    copies = jnp.broadcast_to(part[None], (rows,) + part.shape)
    part = lax.all_to_all(copies, "gy", 0, 0, tiled=True).sum(0)
    spread_out = jnp.broadcast_to(part[None], (count,) + part.shape)
    return lax.all_to_all(spread_out, "gx", 0, 0, tiled=True).reshape(values.shape)


def pad_sides(field, width):
    return jnp.pad(field, [(0, 0)] * (field.ndim - 2) + [(width, width), (width, width)])


def local(
    diffusivity,
    base_humidity,
    coupling,
    basis_rows,
    basis_cols,
    directions,
    send_cell,
    send_weight,
    send_count,
    owner_gauge,
    noise_precision,
):
    rim_depth = STEPS
    reach = rim_depth + 1
    height, breadth = diffusivity.shape
    n_dirs = directions.shape[0]
    static = jnp.stack([diffusivity, base_humidity, coupling, jnp.ones_like(diffusivity)])
    static_gx, rows_wide = exchange(((static, 1), (basis_rows, 0)), "gx", reach)
    static_wide, cols_wide = exchange(((static_gx, 2), (basis_cols, 0)), "gy", reach)
    static_six = window(static_wide, reach, rim_depth)
    rows_six = rows_wide[1:-1]
    cols_six = cols_wide[1:-1]
    perturb = jnp.einsum("xa,rab->rxb", rows_six, directions, precision=exact)
    perturb = jnp.einsum("rxb,yb->rxy", perturb, cols_six, precision=exact)
    param_wide = static_six[0] * perturb
    source = make_source(param_wide, static_six)
    src_depth = rim_depth - 1
    state_now = jnp.stack([jnp.zeros_like(source), step_ratio * source])
    for i in range(rim_depth - 1):
        depth = src_depth - i
        state_now = advance(state_now, window(static_wide, reach, depth), 1.0)
        state_now = jnp.stack(
            [state_now[0], state_now[1] + step_ratio * window(source, src_depth, depth - 1)]
        )
    humid = state_now[1]
    peers = send_cell.shape[2]
    slots = send_cell.shape[3]
    gauges = noise_precision.shape[2]
    cell_ids = send_cell.reshape(-1)
    live_mask = (
        lax.broadcasted_iota(jnp.int32, (peers, slots), 1) < send_count.reshape(peers, 1)
    ).astype(jnp.float32)
    factor = send_weight.reshape(peers, slots) * live_mask
    picked = (
        jnp.take(humid.reshape(n_dirs, height * breadth), cell_ids, axis=1).reshape(
            n_dirs, peers, slots
        )
        * factor
    )
    gauge_ids = owner_gauge.reshape(-1)
    lookup = (gauge_ids[:, None] == lax.broadcasted_iota(jnp.int32, (1, gauges), 1)).astype(
        jnp.float32
    )
    gauge_weights = noise_precision.reshape(1, gauges)
    arrived = lax.all_to_all(picked, "gx", split_axis=1, concat_axis=1, tiled=True)
    n_items = arrived.shape[0]
    gauge_read = jnp.dot(arrived.reshape(n_items, peers * slots), lookup, precision=exact)
    backward = jnp.dot(gauge_read * gauge_weights, lookup.T, precision=exact).reshape(
        n_items, peers, slots
    )
    returned = lax.all_to_all(backward, "gx", split_axis=1, concat_axis=1, tiled=True)
    load_values = (returned * factor).reshape(n_dirs, peers * slots)
    adjoint_load = (
        jnp.zeros((n_dirs, height * breadth), jnp.float32).at[:, cell_ids].add(load_values)
    )
    load_wide = pad_sides(adjoint_load.reshape(n_dirs, height, breadth), rim_depth)
    state_now = jnp.stack([jnp.zeros_like(load_wide), load_wide])
    summed = load_wide
    for i in range(rim_depth - 1):
        state_now = pad_sides(advance(state_now, static_six, -1.0), 1)
        summed = summed + state_now[1]
    lam_wide = pad_sides(step_ratio * summed, 1)
    lam_mid, lam_near = spread(lam_wide)
    hum_mid, hum_near = spread(static_wide[1])
    gradient = static_six[0] * sum(
        (0.5 * (h - hum_mid) * (lam_mid - l) for h, l in zip(hum_near, lam_near))
    )
    projected = jnp.einsum("rxy,yb->rxb", gradient, cols_six, precision=exact)
    projected = jnp.einsum("xa,rxb->rab", rows_six, projected, precision=exact)
    summed_modes = all_sum(projected.reshape(n_dirs, -1))
    hess_action = directions + summed_modes.reshape(directions.shape)
    return (gauge_read.reshape(1, 1, n_dirs, gauges), hess_action)


def solution(mesh):
    placed = (
        P("gx", "gy"),
        P("gx", "gy"),
        P("gx", "gy"),
        P("gx", None),
        P("gy", None),
        P(),
        P("gx", "gy", None, None),
        P("gx", "gy", None, None),
        P("gx", "gy", None),
        P("gx", "gy", None, None),
        P("gx", "gy", None),
    )
    return jax.shard_map(
        local,
        mesh=mesh,
        in_specs=placed,
        out_specs=(P("gx", "gy", None, None), P()),
        check_vma=False,
    )
```

```python
import jax
import jax.numpy as jnp
from jax import lax
from jax.sharding import PartitionSpec as P

STEPS = 6


step_ratio = 0.2
exact = lax.Precision.HIGHEST


def extended(cells, sides, width):
    for axis, dim in sides:
        count = lax.axis_size(axis)
        ends = count - 1
        head = lax.slice_in_dim(cells, 0, width, axis=dim)
        tail = lax.slice_in_dim(cells, cells.shape[dim] - width, cells.shape[dim], axis=dim)
        cells = jnp.concatenate(
            [
                lax.ppermute(tail, axis, [(i, (i + 1) % count) for i in range(ends)]),
                cells,
                lax.ppermute(head, axis, [((i + 1) % count, i) for i in range(ends)]),
            ],
            axis=dim,
        )
    return cells


def spread(field):
    middle = field[..., 1:-1, 1:-1]
    return (
        middle,
        (field[..., :-2, 1:-1], field[..., 2:, 1:-1], field[..., 1:-1, :-2], field[..., 1:-1, 2:]),
    )


def window(field, have, want):
    offset = have - want
    return field[..., offset : field.shape[-2] - offset, offset : field.shape[-1] - offset]


def advance(state_now, static_pad, orient):
    temp_mid, temp_near = spread(state_now[0])
    hum_mid, hum_near = spread(state_now[1])
    diff_mid, diff_near = spread(static_pad[0])
    couple_mid = static_pad[2, 1:-1, 1:-1]
    inside = static_pad[3, 1:-1, 1:-1]
    lap_temp = sum((n - temp_mid for n in temp_near))
    lap_hum = sum((0.5 * (diff_mid + k) * (n - hum_mid) for k, n in zip(diff_near, hum_near)))
    new_temp = temp_mid + step_ratio * lap_temp + orient * couple_mid * hum_mid
    new_hum = hum_mid + step_ratio * lap_hum - orient * couple_mid * temp_mid
    return jnp.stack([new_temp * inside, new_hum * inside])


def make_source(param_pad, static_pad):
    param_mid, param_near = spread(param_pad)
    hum_mid, hum_near = spread(static_pad[1])
    inside = static_pad[3, 1:-1, 1:-1]
    return (
        sum((0.5 * (param_mid + p) * (h - hum_mid) for p, h in zip(param_near, hum_near))) * inside
    )


def state_rim(state_now):
    return extended(state_now, (("gx", 2), ("gy", 3)), 1)


def exchange(parts, axis, width):
    count = lax.axis_size(axis)
    ends = count - 1
    heads = [lax.slice_in_dim(a, 0, width, axis=d) for a, d in parts]
    tails = [lax.slice_in_dim(a, a.shape[d] - width, a.shape[d], axis=d) for a, d in parts]

    def pack(pieces):
        return jnp.concatenate([p.reshape(-1) for p in pieces])

    def unpack(flat, like):
        out, offset = [], 0
        for p in like:
            out.append(flat[offset : offset + p.size].reshape(p.shape))
            offset += p.size
        return out

    from_prev = unpack(lax.ppermute(pack(tails), axis, [(i, i + 1) for i in range(ends)]), tails)
    from_next = unpack(lax.ppermute(pack(heads), axis, [(i + 1, i) for i in range(ends)]), heads)
    return [
        jnp.concatenate([p, a, n], axis=d) for (a, d), p, n in zip(parts, from_prev, from_next)
    ]


def all_sum(values):
    count = lax.axis_size("gx")
    rows = lax.axis_size("gy")
    flat = values.reshape(count, -1, 128)
    part = lax.all_to_all(flat, "gx", 0, 0, tiled=True).sum(0)
    copies = jnp.broadcast_to(part[None], (rows,) + part.shape)
    part = lax.all_to_all(copies, "gy", 0, 0, tiled=True).sum(0)
    spread_out = jnp.broadcast_to(part[None], (count,) + part.shape)
    return lax.all_to_all(spread_out, "gx", 0, 0, tiled=True).reshape(values.shape)


def pad_sides(field, width):
    return jnp.pad(field, [(0, 0)] * (field.ndim - 2) + [(width, width), (width, width)])


def neighbours(field):
    rows, cols = field.shape[-2:]
    lead = [(0, 0)] * (field.ndim - 2)
    return (
        jnp.pad(field[..., : rows - 1, :], lead + [(1, 0), (0, 0)]),
        jnp.pad(field[..., 1:, :], lead + [(0, 1), (0, 0)]),
        jnp.pad(field[..., :, : cols - 1], lead + [(0, 0), (1, 0)]),
        jnp.pad(field[..., :, 1:], lead + [(0, 0), (0, 1)]),
    )


def adjoint_projection(adjoint_load, static_six, rows_six, cols_six, depth):
    n_dirs = adjoint_load.shape[0]
    load_wide = pad_sides(adjoint_load, depth)
    tall, wide = load_wide.shape[1:]
    load_flat = jnp.transpose(load_wide, (1, 0, 2)).reshape(tall, n_dirs * wide)
    ring = pad_sides(jnp.ones((tall - 2, wide - 2), jnp.float32), 1)
    fields = jnp.tile(jnp.concatenate([static_six, ring[None]]), (1, 1, n_dirs))
    diff, humid, couple = fields[0], fields[1], fields[2]
    keep = fields[3] * fields[4]
    diff_near = neighbours(diff)
    temper = jnp.zeros_like(load_flat)
    moist = load_flat
    summed = load_flat
    for i in range(depth - 1):
        lap_temp = sum((n - temper for n in neighbours(temper)))
        lap_hum = sum(
            (0.5 * (diff + k) * (n - moist) for k, n in zip(diff_near, neighbours(moist)))
        )
        temper, moist = (
            (temper + step_ratio * lap_temp - couple * moist) * keep,
            (moist + step_ratio * lap_hum + couple * temper) * keep,
        )
        summed = summed + moist
    lam = step_ratio * summed
    gradient = diff * sum(
        (0.5 * (h - humid) * (lam - l) for h, l in zip(neighbours(humid), neighbours(lam)))
    )
    gradient = gradient.reshape(tall, n_dirs, wide)
    projected = jnp.einsum("xry,yb->rxb", gradient, cols_six, precision=exact)
    return jnp.einsum("xa,rxb->rab", rows_six, projected, precision=exact)


def local(
    diffusivity,
    base_humidity,
    coupling,
    basis_rows,
    basis_cols,
    directions,
    send_cell,
    send_weight,
    send_count,
    owner_gauge,
    noise_precision,
):
    rim_depth = STEPS
    reach = rim_depth + 1
    height, breadth = diffusivity.shape
    n_dirs = directions.shape[0]
    static = jnp.stack([diffusivity, base_humidity, coupling, jnp.ones_like(diffusivity)])
    static_gx, rows_wide = exchange(((static, 1), (basis_rows, 0)), "gx", reach)
    static_wide, cols_wide = exchange(((static_gx, 2), (basis_cols, 0)), "gy", reach)
    static_six = window(static_wide, reach, rim_depth)
    rows_six = rows_wide[1:-1]
    cols_six = cols_wide[1:-1]
    perturb = jnp.einsum("xa,rab->rxb", rows_six, directions, precision=exact)
    perturb = jnp.einsum("rxb,yb->rxy", perturb, cols_six, precision=exact)
    param_wide = static_six[0] * perturb
    source = make_source(param_wide, static_six)
    src_depth = rim_depth - 1
    state_now = jnp.stack([jnp.zeros_like(source), step_ratio * source])
    for i in range(rim_depth - 1):
        depth = src_depth - i
        state_now = advance(state_now, window(static_wide, reach, depth), 1.0)
        state_now = jnp.stack(
            [state_now[0], state_now[1] + step_ratio * window(source, src_depth, depth - 1)]
        )
    humid = state_now[1]
    peers = send_cell.shape[2]
    slots = send_cell.shape[3]
    gauges = noise_precision.shape[2]
    cell_ids = send_cell.reshape(-1)
    live_mask = (
        lax.broadcasted_iota(jnp.int32, (peers, slots), 1) < send_count.reshape(peers, 1)
    ).astype(jnp.float32)
    factor = send_weight.reshape(peers, slots) * live_mask
    picked = (
        jnp.take(humid.reshape(n_dirs, height * breadth), cell_ids, axis=1).reshape(
            n_dirs, peers, slots
        )
        * factor
    )
    gauge_ids = owner_gauge.reshape(-1)
    lookup = (gauge_ids[:, None] == lax.broadcasted_iota(jnp.int32, (1, gauges), 1)).astype(
        jnp.float32
    )
    gauge_weights = noise_precision.reshape(1, gauges)
    arrived = lax.all_to_all(picked, "gx", split_axis=1, concat_axis=1, tiled=True)
    n_items = arrived.shape[0]
    gauge_read = jnp.dot(arrived.reshape(n_items, peers * slots), lookup, precision=exact)
    backward = jnp.dot(gauge_read * gauge_weights, lookup.T, precision=exact).reshape(
        n_items, peers, slots
    )
    returned = lax.all_to_all(backward, "gx", split_axis=1, concat_axis=1, tiled=True)
    load_values = (returned * factor).reshape(n_dirs, peers * slots)
    adjoint_load = (
        jnp.zeros((n_dirs, height * breadth), jnp.float32).at[:, cell_ids].add(load_values)
    )
    projected = adjoint_projection(
        adjoint_load.reshape(n_dirs, height, breadth), static_six, rows_six, cols_six, rim_depth
    )
    summed_modes = all_sum(projected.reshape(n_dirs, -1))
    hess_action = directions + summed_modes.reshape(directions.shape)
    return (gauge_read.reshape(1, 1, n_dirs, gauges), hess_action)


def solution(mesh):
    placed = (
        P("gx", "gy"),
        P("gx", "gy"),
        P("gx", "gy"),
        P("gx", None),
        P("gy", None),
        P(),
        P("gx", "gy", None, None),
        P("gx", "gy", None, None),
        P("gx", "gy", None),
        P("gx", "gy", None, None),
        P("gx", "gy", None),
    )
    return jax.shard_map(
        local,
        mesh=mesh,
        in_specs=placed,
        out_specs=(P("gx", "gy", None, None), P()),
        check_vma=False,
    )
```

```python
import jax
import jax.numpy as jnp
from jax import lax
from jax.sharding import PartitionSpec as P

STEPS = 6


step_ratio = 0.2
exact = lax.Precision.HIGHEST


def extended(cells, sides, width):
    for axis, dim in sides:
        count = lax.axis_size(axis)
        ends = count - 1
        head = lax.slice_in_dim(cells, 0, width, axis=dim)
        tail = lax.slice_in_dim(cells, cells.shape[dim] - width, cells.shape[dim], axis=dim)
        cells = jnp.concatenate(
            [
                lax.ppermute(tail, axis, [(i, (i + 1) % count) for i in range(ends)]),
                cells,
                lax.ppermute(head, axis, [((i + 1) % count, i) for i in range(ends)]),
            ],
            axis=dim,
        )
    return cells


def spread(field):
    middle = field[..., 1:-1, 1:-1]
    return (
        middle,
        (field[..., :-2, 1:-1], field[..., 2:, 1:-1], field[..., 1:-1, :-2], field[..., 1:-1, 2:]),
    )


def window(field, have, want):
    offset = have - want
    return field[..., offset : field.shape[-2] - offset, offset : field.shape[-1] - offset]


def advance(state_now, static_pad, orient):
    temp_mid, temp_near = spread(state_now[0])
    hum_mid, hum_near = spread(state_now[1])
    diff_mid, diff_near = spread(static_pad[0])
    couple_mid = static_pad[2, 1:-1, 1:-1]
    inside = static_pad[3, 1:-1, 1:-1]
    lap_temp = sum((n - temp_mid for n in temp_near))
    lap_hum = sum((0.5 * (diff_mid + k) * (n - hum_mid) for k, n in zip(diff_near, hum_near)))
    new_temp = temp_mid + step_ratio * lap_temp + orient * couple_mid * hum_mid
    new_hum = hum_mid + step_ratio * lap_hum - orient * couple_mid * temp_mid
    return jnp.stack([new_temp * inside, new_hum * inside])


def make_source(param_pad, static_pad):
    param_mid, param_near = spread(param_pad)
    hum_mid, hum_near = spread(static_pad[1])
    inside = static_pad[3, 1:-1, 1:-1]
    return (
        sum((0.5 * (param_mid + p) * (h - hum_mid) for p, h in zip(param_near, hum_near))) * inside
    )


def state_rim(state_now):
    return extended(state_now, (("gx", 2), ("gy", 3)), 1)


def exchange(parts, axis, width):
    count = lax.axis_size(axis)
    ends = count - 1
    heads = [lax.slice_in_dim(a, 0, width, axis=d) for a, d in parts]
    tails = [lax.slice_in_dim(a, a.shape[d] - width, a.shape[d], axis=d) for a, d in parts]

    def pack(pieces):
        return jnp.concatenate([p.reshape(-1) for p in pieces])

    def unpack(flat, like):
        out, offset = [], 0
        for p in like:
            out.append(flat[offset : offset + p.size].reshape(p.shape))
            offset += p.size
        return out

    from_prev = unpack(lax.ppermute(pack(tails), axis, [(i, i + 1) for i in range(ends)]), tails)
    from_next = unpack(lax.ppermute(pack(heads), axis, [(i + 1, i) for i in range(ends)]), heads)
    return [
        jnp.concatenate([p, a, n], axis=d) for (a, d), p, n in zip(parts, from_prev, from_next)
    ]


def all_sum(values):
    count = lax.axis_size("gx")
    rows = lax.axis_size("gy")
    flat = values.reshape(count, -1, 128)
    part = lax.all_to_all(flat, "gx", 0, 0, tiled=True).sum(0)
    copies = jnp.broadcast_to(part[None], (rows,) + part.shape)
    part = lax.all_to_all(copies, "gy", 0, 0, tiled=True).sum(0)
    spread_out = jnp.broadcast_to(part[None], (count,) + part.shape)
    return lax.all_to_all(spread_out, "gx", 0, 0, tiled=True).reshape(values.shape)


def pad_sides(field, width):
    return jnp.pad(field, [(0, 0)] * (field.ndim - 2) + [(width, width), (width, width)])


def neighbours(field):
    rows, cols = field.shape[-2:]
    lead = [(0, 0)] * (field.ndim - 2)
    return (
        jnp.pad(field[..., : rows - 1, :], lead + [(1, 0), (0, 0)]),
        jnp.pad(field[..., 1:, :], lead + [(0, 1), (0, 0)]),
        jnp.pad(field[..., :, : cols - 1], lead + [(0, 0), (1, 0)]),
        jnp.pad(field[..., :, 1:], lead + [(0, 0), (0, 1)]),
    )


def adjoint_projection(adjoint_load, static_six, rows_six, cols_six, depth):
    load_wide = pad_sides(adjoint_load, depth)
    tall, wide = load_wide.shape[1:]
    ring = pad_sides(jnp.ones((tall - 2, wide - 2), jnp.float32), 1)
    diff, humid, couple = static_six[0], static_six[1], static_six[2]
    keep = static_six[3] * ring
    diff_near = neighbours(diff)
    temper = jnp.zeros_like(load_wide)
    moist = load_wide
    summed = load_wide
    for i in range(depth - 1):
        lap_temp = sum((n - temper for n in neighbours(temper)))
        lap_hum = sum(
            (0.5 * (diff + k) * (n - moist) for k, n in zip(diff_near, neighbours(moist)))
        )
        temper, moist = (
            (temper + step_ratio * lap_temp - couple * moist) * keep,
            (moist + step_ratio * lap_hum + couple * temper) * keep,
        )
        summed = summed + moist
    lam = step_ratio * summed
    gradient = diff * sum(
        (0.5 * (h - humid) * (lam - l) for h, l in zip(neighbours(humid), neighbours(lam)))
    )
    projected = jnp.einsum("rxy,yb->rxb", gradient, cols_six, precision=exact)
    return jnp.einsum("xa,rxb->rab", rows_six, projected, precision=exact)


def local(
    diffusivity,
    base_humidity,
    coupling,
    basis_rows,
    basis_cols,
    directions,
    send_cell,
    send_weight,
    send_count,
    owner_gauge,
    noise_precision,
):
    rim_depth = STEPS
    reach = rim_depth + 1
    height, breadth = diffusivity.shape
    n_dirs = directions.shape[0]
    static = jnp.stack([diffusivity, base_humidity, coupling, jnp.ones_like(diffusivity)])
    static_gx, rows_wide = exchange(((static, 1), (basis_rows, 0)), "gx", reach)
    static_wide, cols_wide = exchange(((static_gx, 2), (basis_cols, 0)), "gy", reach)
    static_six = window(static_wide, reach, rim_depth)
    rows_six = rows_wide[1:-1]
    cols_six = cols_wide[1:-1]
    perturb = jnp.einsum("xa,rab->rxb", rows_six, directions, precision=exact)
    perturb = jnp.einsum("rxb,yb->rxy", perturb, cols_six, precision=exact)
    param_wide = static_six[0] * perturb
    source = make_source(param_wide, static_six)
    src_depth = rim_depth - 1
    state_now = jnp.stack([jnp.zeros_like(source), step_ratio * source])
    for i in range(rim_depth - 1):
        depth = src_depth - i
        state_now = advance(state_now, window(static_wide, reach, depth), 1.0)
        state_now = jnp.stack(
            [state_now[0], state_now[1] + step_ratio * window(source, src_depth, depth - 1)]
        )
    humid = state_now[1]
    peers = send_cell.shape[2]
    slots = send_cell.shape[3]
    gauges = noise_precision.shape[2]
    cell_ids = send_cell.reshape(-1)
    live_mask = (
        lax.broadcasted_iota(jnp.int32, (peers, slots), 1) < send_count.reshape(peers, 1)
    ).astype(jnp.float32)
    factor = send_weight.reshape(peers, slots) * live_mask
    picked = (
        jnp.take(humid.reshape(n_dirs, height * breadth), cell_ids, axis=1).reshape(
            n_dirs, peers, slots
        )
        * factor
    )
    gauge_ids = owner_gauge.reshape(-1)
    lookup = (gauge_ids[:, None] == lax.broadcasted_iota(jnp.int32, (1, gauges), 1)).astype(
        jnp.float32
    )
    gauge_weights = noise_precision.reshape(1, gauges)
    arrived = lax.all_to_all(picked, "gx", split_axis=1, concat_axis=1, tiled=True)
    n_items = arrived.shape[0]
    gauge_read = jnp.dot(arrived.reshape(n_items, peers * slots), lookup, precision=exact)
    backward = jnp.dot(gauge_read * gauge_weights, lookup.T, precision=exact).reshape(
        n_items, peers, slots
    )
    returned = lax.all_to_all(backward, "gx", split_axis=1, concat_axis=1, tiled=True)
    load_values = (returned * factor).reshape(n_dirs, peers * slots)
    adjoint_load = (
        jnp.zeros((n_dirs, height * breadth), jnp.float32).at[:, cell_ids].add(load_values)
    )
    projected = adjoint_projection(
        adjoint_load.reshape(n_dirs, height, breadth), static_six, rows_six, cols_six, rim_depth
    )
    summed_modes = all_sum(projected.reshape(n_dirs, -1))
    hess_action = directions + summed_modes.reshape(directions.shape)
    return (gauge_read.reshape(1, 1, n_dirs, gauges), hess_action)


def solution(mesh):
    placed = (
        P("gx", "gy"),
        P("gx", "gy"),
        P("gx", "gy"),
        P("gx", None),
        P("gy", None),
        P(),
        P("gx", "gy", None, None),
        P("gx", "gy", None, None),
        P("gx", "gy", None),
        P("gx", "gy", None, None),
        P("gx", "gy", None),
    )
    return jax.shard_map(
        local,
        mesh=mesh,
        in_specs=placed,
        out_specs=(P("gx", "gy", None, None), P()),
        check_vma=False,
    )
```

```python
import jax
import jax.numpy as jnp
from jax import lax
from jax.sharding import PartitionSpec as P

STEPS = 6


step_ratio = 0.2
exact = lax.Precision.HIGHEST


def extended(cells, sides, width):
    for axis, dim in sides:
        count = lax.axis_size(axis)
        ends = count - 1
        head = lax.slice_in_dim(cells, 0, width, axis=dim)
        tail = lax.slice_in_dim(cells, cells.shape[dim] - width, cells.shape[dim], axis=dim)
        cells = jnp.concatenate(
            [
                lax.ppermute(tail, axis, [(i, (i + 1) % count) for i in range(ends)]),
                cells,
                lax.ppermute(head, axis, [((i + 1) % count, i) for i in range(ends)]),
            ],
            axis=dim,
        )
    return cells


def spread(field):
    middle = field[..., 1:-1, 1:-1]
    return (
        middle,
        (field[..., :-2, 1:-1], field[..., 2:, 1:-1], field[..., 1:-1, :-2], field[..., 1:-1, 2:]),
    )


def window(field, have, want):
    offset = have - want
    return field[..., offset : field.shape[-2] - offset, offset : field.shape[-1] - offset]


def advance(state_now, static_pad, orient):
    temp_mid, temp_near = spread(state_now[0])
    hum_mid, hum_near = spread(state_now[1])
    diff_mid, diff_near = spread(static_pad[0])
    couple_mid = static_pad[2, 1:-1, 1:-1]
    inside = static_pad[3, 1:-1, 1:-1]
    lap_temp = sum((n - temp_mid for n in temp_near))
    lap_hum = sum((0.5 * (diff_mid + k) * (n - hum_mid) for k, n in zip(diff_near, hum_near)))
    new_temp = temp_mid + step_ratio * lap_temp + orient * couple_mid * hum_mid
    new_hum = hum_mid + step_ratio * lap_hum - orient * couple_mid * temp_mid
    return jnp.stack([new_temp * inside, new_hum * inside])


def make_source(param_pad, static_pad):
    param_mid, param_near = spread(param_pad)
    hum_mid, hum_near = spread(static_pad[1])
    inside = static_pad[3, 1:-1, 1:-1]
    return (
        sum((0.5 * (param_mid + p) * (h - hum_mid) for p, h in zip(param_near, hum_near))) * inside
    )


def state_rim(state_now):
    return extended(state_now, (("gx", 2), ("gy", 3)), 1)


def exchange(parts, axis, width):
    count = lax.axis_size(axis)
    ends = count - 1
    heads = [lax.slice_in_dim(a, 0, width, axis=d) for a, d in parts]
    tails = [lax.slice_in_dim(a, a.shape[d] - width, a.shape[d], axis=d) for a, d in parts]

    def pack(pieces):
        return jnp.concatenate([p.reshape(-1) for p in pieces])

    def unpack(flat, like):
        out, offset = [], 0
        for p in like:
            out.append(flat[offset : offset + p.size].reshape(p.shape))
            offset += p.size
        return out

    from_prev = unpack(lax.ppermute(pack(tails), axis, [(i, i + 1) for i in range(ends)]), tails)
    from_next = unpack(lax.ppermute(pack(heads), axis, [(i + 1, i) for i in range(ends)]), heads)
    return [
        jnp.concatenate([p, a, n], axis=d) for (a, d), p, n in zip(parts, from_prev, from_next)
    ]


def all_sum(values):
    count = lax.axis_size("gx")
    rows = lax.axis_size("gy")
    flat = values.reshape(count, -1, 128)
    part = lax.all_to_all(flat, "gx", 0, 0, tiled=True).sum(0)
    copies = jnp.broadcast_to(part[None], (rows,) + part.shape)
    part = lax.all_to_all(copies, "gy", 0, 0, tiled=True).sum(0)
    spread_out = jnp.broadcast_to(part[None], (count,) + part.shape)
    return lax.all_to_all(spread_out, "gx", 0, 0, tiled=True).reshape(values.shape)


def pad_sides(field, width):
    return jnp.pad(field, [(0, 0)] * (field.ndim - 2) + [(width, width), (width, width)])


def local(
    diffusivity,
    base_humidity,
    coupling,
    basis_rows,
    basis_cols,
    directions,
    send_cell,
    send_weight,
    send_count,
    owner_gauge,
    noise_precision,
):
    rim_depth = STEPS
    reach = rim_depth + 1
    height, breadth = diffusivity.shape
    n_dirs = directions.shape[0]
    static = jnp.stack([diffusivity, base_humidity, coupling])
    static_gy, cols_wide = exchange(((static, 2), (basis_cols, 0)), "gy", reach)
    static_both, rows_wide = exchange(((static_gy, 1), (basis_rows, 0)), "gx", reach)
    row_at = lax.axis_index("gx") * height - reach + lax.broadcasted_iota(
        jnp.int32, (height + 2 * reach, breadth + 2 * reach), 0
    )
    col_at = lax.axis_index("gy") * breadth - reach + lax.broadcasted_iota(
        jnp.int32, (height + 2 * reach, breadth + 2 * reach), 1
    )
    inside_grid = (
        (row_at >= 0)
        & (row_at < height * lax.axis_size("gx"))
        & (col_at >= 0)
        & (col_at < breadth * lax.axis_size("gy"))
    ).astype(jnp.float32)
    static_wide = jnp.concatenate([static_both, inside_grid[None]])
    static_six = window(static_wide, reach, rim_depth)
    rows_six = rows_wide[1:-1]
    cols_six = cols_wide[1:-1]
    perturb = jnp.einsum("xa,rab->rxb", rows_six, directions, precision=exact)
    perturb = jnp.einsum("rxb,yb->rxy", perturb, cols_six, precision=exact)
    param_wide = static_six[0] * perturb
    source = make_source(param_wide, static_six)
    src_depth = rim_depth - 1
    state_now = jnp.stack([jnp.zeros_like(source), step_ratio * source])
    for i in range(rim_depth - 1):
        depth = src_depth - i
        state_now = advance(state_now, window(static_wide, reach, depth), 1.0)
        state_now = jnp.stack(
            [state_now[0], state_now[1] + step_ratio * window(source, src_depth, depth - 1)]
        )
    humid = state_now[1]
    peers = send_cell.shape[2]
    slots = send_cell.shape[3]
    gauges = noise_precision.shape[2]
    cell_ids = send_cell.reshape(-1)
    live_mask = (
        lax.broadcasted_iota(jnp.int32, (peers, slots), 1) < send_count.reshape(peers, 1)
    ).astype(jnp.float32)
    factor = send_weight.reshape(peers, slots) * live_mask
    picked = (
        jnp.take(humid.reshape(n_dirs, height * breadth), cell_ids, axis=1).reshape(
            n_dirs, peers, slots
        )
        * factor
    )
    gauge_ids = owner_gauge.reshape(-1)
    lookup = (gauge_ids[:, None] == lax.broadcasted_iota(jnp.int32, (1, gauges), 1)).astype(
        jnp.float32
    )
    gauge_weights = noise_precision.reshape(1, gauges)
    arrived = lax.all_to_all(picked, "gx", split_axis=1, concat_axis=1, tiled=True)
    n_items = arrived.shape[0]
    gauge_read = jnp.dot(arrived.reshape(n_items, peers * slots), lookup, precision=exact)
    backward = jnp.dot(gauge_read * gauge_weights, lookup.T, precision=exact).reshape(
        n_items, peers, slots
    )
    returned = lax.all_to_all(backward, "gx", split_axis=1, concat_axis=1, tiled=True)
    load_values = (returned * factor).reshape(n_dirs, peers * slots)
    adjoint_load = (
        jnp.zeros((n_dirs, height * breadth), jnp.float32).at[:, cell_ids].add(load_values)
    )
    load_wide = pad_sides(adjoint_load.reshape(n_dirs, height, breadth), rim_depth)
    state_now = jnp.stack([jnp.zeros_like(load_wide), load_wide])
    summed = load_wide
    for i in range(rim_depth - 1):
        state_now = pad_sides(advance(state_now, static_six, -1.0), 1)
        summed = summed + state_now[1]
    lam_wide = pad_sides(step_ratio * summed, 1)
    lam_mid, lam_near = spread(lam_wide)
    hum_mid, hum_near = spread(static_wide[1])
    gradient = static_six[0] * sum(
        (0.5 * (h - hum_mid) * (lam_mid - l) for h, l in zip(hum_near, lam_near))
    )
    projected = jnp.einsum("rxy,yb->rxb", gradient, cols_six, precision=exact)
    projected = jnp.einsum("xa,rxb->rab", rows_six, projected, precision=exact)
    summed_modes = all_sum(projected.reshape(n_dirs, -1))
    hess_action = directions + summed_modes.reshape(directions.shape)
    return (gauge_read.reshape(1, 1, n_dirs, gauges), hess_action)


def solution(mesh):
    placed = (
        P("gx", "gy"),
        P("gx", "gy"),
        P("gx", "gy"),
        P("gx", None),
        P("gy", None),
        P(),
        P("gx", "gy", None, None),
        P("gx", "gy", None, None),
        P("gx", "gy", None),
        P("gx", "gy", None, None),
        P("gx", "gy", None),
    )
    return jax.shard_map(
        local,
        mesh=mesh,
        in_specs=placed,
        out_specs=(P("gx", "gy", None, None), P()),
        check_vma=False,
    )
```

```python
import jax
import jax.numpy as jnp
from jax import lax
from jax.sharding import PartitionSpec as P

STEPS = 6


step_ratio = 0.2
exact = lax.Precision.HIGHEST


def extended(cells, sides, width):
    for axis, dim in sides:
        count = lax.axis_size(axis)
        ends = count - 1
        head = lax.slice_in_dim(cells, 0, width, axis=dim)
        tail = lax.slice_in_dim(cells, cells.shape[dim] - width, cells.shape[dim], axis=dim)
        cells = jnp.concatenate(
            [
                lax.ppermute(tail, axis, [(i, (i + 1) % count) for i in range(ends)]),
                cells,
                lax.ppermute(head, axis, [((i + 1) % count, i) for i in range(ends)]),
            ],
            axis=dim,
        )
    return cells


def spread(field):
    middle = field[..., 1:-1, 1:-1]
    return (
        middle,
        (field[..., :-2, 1:-1], field[..., 2:, 1:-1], field[..., 1:-1, :-2], field[..., 1:-1, 2:]),
    )


def window(field, have, want):
    offset = have - want
    return field[..., offset : field.shape[-2] - offset, offset : field.shape[-1] - offset]


def advance(state_now, static_pad, orient):
    temp_mid, temp_near = spread(state_now[0])
    hum_mid, hum_near = spread(state_now[1])
    diff_mid, diff_near = spread(static_pad[0])
    couple_mid = static_pad[2, 1:-1, 1:-1]
    inside = static_pad[3, 1:-1, 1:-1]
    lap_temp = sum((n - temp_mid for n in temp_near))
    lap_hum = sum((0.5 * (diff_mid + k) * (n - hum_mid) for k, n in zip(diff_near, hum_near)))
    new_temp = temp_mid + step_ratio * lap_temp + orient * couple_mid * hum_mid
    new_hum = hum_mid + step_ratio * lap_hum - orient * couple_mid * temp_mid
    return jnp.stack([new_temp * inside, new_hum * inside])


def make_source(param_pad, static_pad):
    param_mid, param_near = spread(param_pad)
    hum_mid, hum_near = spread(static_pad[1])
    inside = static_pad[3, 1:-1, 1:-1]
    return (
        sum((0.5 * (param_mid + p) * (h - hum_mid) for p, h in zip(param_near, hum_near))) * inside
    )


def state_rim(state_now):
    return extended(state_now, (("gx", 2), ("gy", 3)), 1)


def exchange(parts, axis, width):
    count = lax.axis_size(axis)
    ends = count - 1
    heads = [lax.slice_in_dim(a, 0, width, axis=d) for a, d in parts]
    tails = [lax.slice_in_dim(a, a.shape[d] - width, a.shape[d], axis=d) for a, d in parts]

    def pack(pieces):
        return jnp.concatenate([p.reshape(-1) for p in pieces])

    def unpack(flat, like):
        out, offset = [], 0
        for p in like:
            out.append(flat[offset : offset + p.size].reshape(p.shape))
            offset += p.size
        return out

    from_prev = unpack(lax.ppermute(pack(tails), axis, [(i, i + 1) for i in range(ends)]), tails)
    from_next = unpack(lax.ppermute(pack(heads), axis, [(i + 1, i) for i in range(ends)]), heads)
    return [
        jnp.concatenate([p, a, n], axis=d) for (a, d), p, n in zip(parts, from_prev, from_next)
    ]


def all_sum(values):
    count = lax.axis_size("gx")
    rows = lax.axis_size("gy")
    flat = values.reshape(count, -1, 128)
    part = lax.all_to_all(flat, "gx", 0, 0, tiled=True).sum(0)
    copies = jnp.broadcast_to(part[None], (rows,) + part.shape)
    part = lax.all_to_all(copies, "gy", 0, 0, tiled=True).sum(0)
    spread_out = jnp.broadcast_to(part[None], (count,) + part.shape)
    return lax.all_to_all(spread_out, "gx", 0, 0, tiled=True).reshape(values.shape)


def pad_sides(field, width):
    return jnp.pad(field, [(0, 0)] * (field.ndim - 2) + [(width, width), (width, width)])


def local(
    diffusivity,
    base_humidity,
    coupling,
    basis_rows,
    basis_cols,
    directions,
    send_cell,
    send_weight,
    send_count,
    owner_gauge,
    noise_precision,
):
    rim_depth = STEPS
    reach = rim_depth + 1
    height, breadth = diffusivity.shape
    n_dirs = directions.shape[0]
    static = jnp.stack([diffusivity, base_humidity, coupling, jnp.ones_like(diffusivity)])
    static_gx, rows_wide = exchange(((static, 1), (basis_rows, 0)), "gx", reach)
    static_wide, cols_wide = exchange(((static_gx, 2), (basis_cols, 0)), "gy", reach)
    static_six = window(static_wide, reach, rim_depth)
    rows_six = rows_wide[1:-1]
    cols_six = cols_wide[1:-1]
    perturb = jnp.einsum("xa,rab->rxb", rows_six, directions, precision=exact)
    perturb = jnp.einsum("rxb,yb->rxy", perturb, cols_six, precision=exact)
    param_wide = static_six[0] * perturb
    source = make_source(param_wide, static_six)
    src_depth = rim_depth - 1
    state_now = jnp.stack([jnp.zeros_like(source), step_ratio * source])
    for i in range(rim_depth - 1):
        depth = src_depth - i
        state_now = advance(state_now, window(static_wide, reach, depth), 1.0)
        state_now = jnp.stack(
            [state_now[0], state_now[1] + step_ratio * window(source, src_depth, depth - 1)]
        )
    humid = state_now[1]
    peers = send_cell.shape[2]
    slots = send_cell.shape[3]
    gauges = noise_precision.shape[2]
    cell_ids = send_cell.reshape(-1)
    live_mask = (
        lax.broadcasted_iota(jnp.int32, (peers, slots), 1) < send_count.reshape(peers, 1)
    ).astype(jnp.float32)
    factor = send_weight.reshape(peers, slots) * live_mask
    select = (
        cell_ids[:, None] == lax.broadcasted_iota(jnp.int32, (1, height * breadth), 1)
    ).astype(jnp.float32)
    picked = (
        jnp.take(humid.reshape(n_dirs, height * breadth), cell_ids, axis=1).reshape(
            n_dirs, peers, slots
        )
        * factor
    )
    gauge_ids = owner_gauge.reshape(-1)
    lookup = (gauge_ids[:, None] == lax.broadcasted_iota(jnp.int32, (1, gauges), 1)).astype(
        jnp.float32
    )
    gauge_weights = noise_precision.reshape(1, gauges)
    arrived = lax.all_to_all(picked, "gx", split_axis=1, concat_axis=1, tiled=True)
    n_items = arrived.shape[0]
    gauge_read = jnp.dot(arrived.reshape(n_items, peers * slots), lookup, precision=exact)
    backward = jnp.dot(gauge_read * gauge_weights, lookup.T, precision=exact).reshape(
        n_items, peers, slots
    )
    returned = lax.all_to_all(backward, "gx", split_axis=1, concat_axis=1, tiled=True)
    load_values = (returned * factor).reshape(n_dirs, peers * slots)
    adjoint_load = jnp.dot(load_values, select, precision=exact)
    load_wide = pad_sides(adjoint_load.reshape(n_dirs, height, breadth), rim_depth)
    state_now = jnp.stack([jnp.zeros_like(load_wide), load_wide])
    summed = load_wide
    for i in range(rim_depth - 1):
        state_now = pad_sides(advance(state_now, static_six, -1.0), 1)
        summed = summed + state_now[1]
    lam_wide = pad_sides(step_ratio * summed, 1)
    lam_mid, lam_near = spread(lam_wide)
    hum_mid, hum_near = spread(static_wide[1])
    gradient = static_six[0] * sum(
        (0.5 * (h - hum_mid) * (lam_mid - l) for h, l in zip(hum_near, lam_near))
    )
    projected = jnp.einsum("rxy,yb->rxb", gradient, cols_six, precision=exact)
    projected = jnp.einsum("xa,rxb->rab", rows_six, projected, precision=exact)
    summed_modes = all_sum(projected.reshape(n_dirs, -1))
    hess_action = directions + summed_modes.reshape(directions.shape)
    return (gauge_read.reshape(1, 1, n_dirs, gauges), hess_action)


def solution(mesh):
    placed = (
        P("gx", "gy"),
        P("gx", "gy"),
        P("gx", "gy"),
        P("gx", None),
        P("gy", None),
        P(),
        P("gx", "gy", None, None),
        P("gx", "gy", None, None),
        P("gx", "gy", None),
        P("gx", "gy", None, None),
        P("gx", "gy", None),
    )
    return jax.shard_map(
        local,
        mesh=mesh,
        in_specs=placed,
        out_specs=(P("gx", "gy", None, None), P()),
        check_vma=False,
    )
```

```python
import jax
import jax.numpy as jnp
from jax import lax
from jax.sharding import PartitionSpec as P

STEPS = 6


step_ratio = 0.2
exact = lax.Precision.HIGHEST


def extended(cells, sides, width):
    for axis, dim in sides:
        count = lax.axis_size(axis)
        ends = count - 1
        head = lax.slice_in_dim(cells, 0, width, axis=dim)
        tail = lax.slice_in_dim(cells, cells.shape[dim] - width, cells.shape[dim], axis=dim)
        cells = jnp.concatenate(
            [
                lax.ppermute(tail, axis, [(i, (i + 1) % count) for i in range(ends)]),
                cells,
                lax.ppermute(head, axis, [((i + 1) % count, i) for i in range(ends)]),
            ],
            axis=dim,
        )
    return cells


def spread(field):
    middle = field[..., 1:-1, 1:-1]
    return (
        middle,
        (field[..., :-2, 1:-1], field[..., 2:, 1:-1], field[..., 1:-1, :-2], field[..., 1:-1, 2:]),
    )


def window(field, have, want):
    offset = have - want
    return field[..., offset : field.shape[-2] - offset, offset : field.shape[-1] - offset]


def advance(state_now, static_pad, orient):
    temp_mid, temp_near = spread(state_now[0])
    hum_mid, hum_near = spread(state_now[1])
    diff_mid, diff_near = spread(static_pad[0])
    couple_mid = static_pad[2, 1:-1, 1:-1]
    inside = static_pad[3, 1:-1, 1:-1]
    lap_temp = sum((n - temp_mid for n in temp_near))
    lap_hum = sum((0.5 * (diff_mid + k) * (n - hum_mid) for k, n in zip(diff_near, hum_near)))
    new_temp = temp_mid + step_ratio * lap_temp + orient * couple_mid * hum_mid
    new_hum = hum_mid + step_ratio * lap_hum - orient * couple_mid * temp_mid
    return jnp.stack([new_temp * inside, new_hum * inside])


def make_source(param_pad, static_pad):
    param_mid, param_near = spread(param_pad)
    hum_mid, hum_near = spread(static_pad[1])
    inside = static_pad[3, 1:-1, 1:-1]
    return (
        sum((0.5 * (param_mid + p) * (h - hum_mid) for p, h in zip(param_near, hum_near))) * inside
    )


def state_rim(state_now):
    return extended(state_now, (("gx", 2), ("gy", 3)), 1)


def exchange(parts, axis, width):
    count = lax.axis_size(axis)
    ends = count - 1
    heads = [lax.slice_in_dim(a, 0, width, axis=d) for a, d in parts]
    tails = [lax.slice_in_dim(a, a.shape[d] - width, a.shape[d], axis=d) for a, d in parts]

    def pack(pieces):
        return jnp.concatenate([p.reshape(-1) for p in pieces])

    def unpack(flat, like):
        out, offset = [], 0
        for p in like:
            out.append(flat[offset : offset + p.size].reshape(p.shape))
            offset += p.size
        return out

    from_prev = unpack(lax.ppermute(pack(tails), axis, [(i, i + 1) for i in range(ends)]), tails)
    from_next = unpack(lax.ppermute(pack(heads), axis, [(i + 1, i) for i in range(ends)]), heads)
    return [
        jnp.concatenate([p, a, n], axis=d) for (a, d), p, n in zip(parts, from_prev, from_next)
    ]


def all_sum(values):
    count = lax.axis_size("gx")
    rows = lax.axis_size("gy")
    flat = values.reshape(count, -1, 128)
    part = lax.all_to_all(flat, "gx", 0, 0, tiled=True).sum(0)
    copies = jnp.broadcast_to(part[None], (rows,) + part.shape)
    part = lax.all_to_all(copies, "gy", 0, 0, tiled=True).sum(0)
    spread_out = jnp.broadcast_to(part[None], (count,) + part.shape)
    return lax.all_to_all(spread_out, "gx", 0, 0, tiled=True).reshape(values.shape)


def pad_sides(field, width):
    return jnp.pad(field, [(0, 0)] * (field.ndim - 2) + [(width, width), (width, width)])


def neighbours(field):
    rows, cols = field.shape[-2:]
    lead = [(0, 0)] * (field.ndim - 2)
    return (
        jnp.pad(field[..., : rows - 1, :], lead + [(1, 0), (0, 0)]),
        jnp.pad(field[..., 1:, :], lead + [(0, 1), (0, 0)]),
        jnp.pad(field[..., :, : cols - 1], lead + [(0, 0), (1, 0)]),
        jnp.pad(field[..., :, 1:], lead + [(0, 0), (0, 1)]),
    )


def adjoint_projection(adjoint_load, static_six, rows_six, cols_six, depth):
    load_wide = pad_sides(adjoint_load, depth)
    tall, wide = load_wide.shape[1:]
    ring = pad_sides(jnp.ones((tall - 2, wide - 2), jnp.float32), 1)
    diff, humid, couple = static_six[0], static_six[1], static_six[2]
    keep = static_six[3] * ring
    diff_near = neighbours(diff)
    temper = jnp.zeros_like(load_wide)
    moist = load_wide
    summed = load_wide
    for i in range(depth - 1):
        lap_temp = sum((n - temper for n in neighbours(temper)))
        lap_hum = sum(
            (0.5 * (diff + k) * (n - moist) for k, n in zip(diff_near, neighbours(moist)))
        )
        temper, moist = (
            (temper + step_ratio * lap_temp - couple * moist) * keep,
            (moist + step_ratio * lap_hum + couple * temper) * keep,
        )
        summed = summed + moist
    lam = step_ratio * summed
    gradient = diff * sum(
        (0.5 * (h - humid) * (lam - l) for h, l in zip(neighbours(humid), neighbours(lam)))
    )
    projected = jnp.einsum("rxy,yb->rxb", gradient, cols_six, precision=exact)
    return jnp.einsum("xa,rxb->rab", rows_six, projected, precision=exact)


def local(
    diffusivity,
    base_humidity,
    coupling,
    basis_rows,
    basis_cols,
    directions,
    send_cell,
    send_weight,
    send_count,
    owner_gauge,
    noise_precision,
):
    rim_depth = STEPS
    reach = rim_depth
    height, breadth = diffusivity.shape
    n_dirs = directions.shape[0]
    static = jnp.stack([diffusivity, base_humidity, coupling, jnp.ones_like(diffusivity)])
    static_gx, rows_wide = exchange(((static, 1), (basis_rows, 0)), "gx", reach)
    static_wide, cols_wide = exchange(((static_gx, 2), (basis_cols, 0)), "gy", reach)
    static_six = static_wide
    rows_six = rows_wide
    cols_six = cols_wide
    perturb = jnp.einsum("xa,rab->rxb", rows_six, directions, precision=exact)
    perturb = jnp.einsum("rxb,yb->rxy", perturb, cols_six, precision=exact)
    param_wide = static_six[0] * perturb
    source = make_source(param_wide, static_six)
    src_depth = rim_depth - 1
    state_now = jnp.stack([jnp.zeros_like(source), step_ratio * source])
    for i in range(rim_depth - 1):
        depth = src_depth - i
        state_now = advance(state_now, window(static_wide, reach, depth), 1.0)
        state_now = jnp.stack(
            [state_now[0], state_now[1] + step_ratio * window(source, src_depth, depth - 1)]
        )
    humid = state_now[1]
    peers = send_cell.shape[2]
    slots = send_cell.shape[3]
    gauges = noise_precision.shape[2]
    cell_ids = send_cell.reshape(-1)
    live_mask = (
        lax.broadcasted_iota(jnp.int32, (peers, slots), 1) < send_count.reshape(peers, 1)
    ).astype(jnp.float32)
    factor = send_weight.reshape(peers, slots) * live_mask
    picked = (
        jnp.take(humid.reshape(n_dirs, height * breadth), cell_ids, axis=1).reshape(
            n_dirs, peers, slots
        )
        * factor
    )
    gauge_ids = owner_gauge.reshape(-1)
    lookup = (gauge_ids[:, None] == lax.broadcasted_iota(jnp.int32, (1, gauges), 1)).astype(
        jnp.float32
    )
    gauge_weights = noise_precision.reshape(1, gauges)
    arrived = lax.all_to_all(picked, "gx", split_axis=1, concat_axis=1, tiled=True)
    n_items = arrived.shape[0]
    gauge_read = jnp.dot(arrived.reshape(n_items, peers * slots), lookup, precision=exact)
    backward = jnp.dot(gauge_read * gauge_weights, lookup.T, precision=exact).reshape(
        n_items, peers, slots
    )
    returned = lax.all_to_all(backward, "gx", split_axis=1, concat_axis=1, tiled=True)
    load_values = (returned * factor).reshape(n_dirs, peers * slots)
    adjoint_load = (
        jnp.zeros((n_dirs, height * breadth), jnp.float32).at[:, cell_ids].add(load_values)
    )
    projected = adjoint_projection(
        adjoint_load.reshape(n_dirs, height, breadth), static_six, rows_six, cols_six, rim_depth
    )
    summed_modes = all_sum(projected.reshape(n_dirs, -1))
    hess_action = directions + summed_modes.reshape(directions.shape)
    return (gauge_read.reshape(1, 1, n_dirs, gauges), hess_action)


def solution(mesh):
    placed = (
        P("gx", "gy"),
        P("gx", "gy"),
        P("gx", "gy"),
        P("gx", None),
        P("gy", None),
        P(),
        P("gx", "gy", None, None),
        P("gx", "gy", None, None),
        P("gx", "gy", None),
        P("gx", "gy", None, None),
        P("gx", "gy", None),
    )
    return jax.shard_map(
        local,
        mesh=mesh,
        in_specs=placed,
        out_specs=(P("gx", "gy", None, None), P()),
        check_vma=False,
    )
```
